512 devices in a mesh: row: 16 (over z), col: 4 (over x_hi, core), depth: 8 (over y, x_lo).
Axes of the slice: x: 4 (x_hi: 2, x_lo: 2; x = x_hi * 2 + x_lo), y: 4, z: 16, core: 2. Of those that a mesh axis runs over, the one named last changes fastest.
Arguments:
- ks_matrix: bfloat16 [4096, 16384], P('col', ('row', 'depth')), may hold values from -6 to 6
- sign_matrix: bfloat16 [16, 8, 128, 12288], P('col', 'depth', None, 'row'), may hold values from -0.046875 to 0.046875
- ks_mask: int32 [32, 128], P('col', ('row', 'depth')), may hold values 0 or 1
- sign_mask: int32 [16, 8, 1, 96], P('col', 'depth', None, 'row'), may hold values 0 or 1
- product_mask: int32 [32, 96], P('col', 'row'), may hold values 0 or 1
- row_order: int32 [4, 8], P('col'), may hold values from 0 to 7, each once within a row
Outputs:
- next_matrix: bfloat16 [4096, 12288], P(('col', 'depth'), 'row')
The draws below stay inside these ranges and needn't reach their ends.
Inputs may be any that keep to these rules, and one draw needn't show every extreme that they name: Each row of row_order names every number of 0 to 7 once.
All inputs are finite; a program needn't handle non-finite values. No bound on the sum of `ks_mask` or of `sign_mask` or of `product_mask` on one device may be relied on, other than what follows from the above.
Results may differ from the reference program's by a relative error of at most 0.001.
Values may be sent and summed in bfloat16 or wider, within the bound.
No kernel may reach another device: no remote copies, remote signals or barrier semaphores. Data moves between devices by JAX's collectives and lax.ppermute only.
A program may use at most 64 MiB of HBM per device.

```python
import jax
import jax.numpy as jnp
from jax import lax

BS = 128
MR = 8
NC = 6
KB = 1
N_ROW = 16
N_COL = 4
N_DEPTH = 8


def place_ends(values, stream_key, least, top_value):
    dims = values.shape
    spot = [jax.random.randint(jax.random.fold_in(stream_key, axis), (), 0, dims[axis]) for axis in range(len(dims))]
    values = values.at[tuple(spot)].set(least)
    longest = dims.index(max(dims))
    spot[longest] = (spot[longest] + 1) % dims[longest]
    return values.at[tuple(spot)].set(top_value)


def shard_levels(rng, extent, shards, low, largest):
    def one(position, blocks):
        heights = jax.random.uniform(jax.random.fold_in(jax.random.fold_in(rng, 6), position), (blocks,), jnp.float32, low / len(shards), largest / len(shards))
        return jnp.repeat(jnp.exp(heights), extent[position] // blocks).reshape((-1,) + (1,) * (len(extent) - position - 1))

    factor_of = one(*shards[0])
    for cut in shards[1:]:
        factor_of = factor_of * one(*cut)
    return factor_of


def scatter_about(key, shape, width, reach, split=(), held_as=jnp.bfloat16):
    level = shard_levels(key, shape, split, -0.22, 0.18) if split else 1.0
    entries = jax.random.normal(key, shape, jnp.float32) * width * level
    return jnp.minimum(jnp.maximum(entries, -reach), reach).astype(held_as)


def setup_inputs(seed: int = 0) -> dict:
    splits = jax.random.split(jax.random.key(seed), 7)
    ks_matrix = scatter_about(splits[0], (MR * N_COL * BS, N_ROW * N_DEPTH * KB * BS), 1.0, 6.0, ((0, 4), (1, 128)))
    sign_matrix = scatter_about(splits[1], (N_ROW, N_DEPTH, KB * BS, NC * N_ROW * BS), (N_ROW * N_DEPTH * KB * BS) ** -0.5, 0.046875, ((0, 4), (1, 8), (3, 16)))
    ks_mask = place_ends((jax.random.randint(splits[2], (MR * N_COL, N_ROW * N_DEPTH * KB), 0, 4) < 3).astype(jnp.int32), jax.random.fold_in(splits[2], 1), 0, 1)
    sign_mask = place_ends((jax.random.randint(splits[3], (N_ROW, N_DEPTH, KB, NC * N_ROW), 0, 4) < 3).astype(jnp.int32), jax.random.fold_in(splits[3], 1), 0, 1)
    product_mask = place_ends((jax.random.randint(splits[4], (MR * N_COL, NC * N_ROW), 0, 4) < 3).astype(jnp.int32), jax.random.fold_in(splits[4], 1), 0, 1)
    row_order = jax.vmap(lambda own: jax.random.permutation(own, MR))(jax.random.split(splits[5], N_COL)).reshape((N_COL, MR)).astype(jnp.int32)
    return dict(ks_matrix=ks_matrix, sign_matrix=sign_matrix, ks_mask=ks_mask, sign_mask=sign_mask, product_mask=product_mask, row_order=row_order)


def reference(ks_matrix, sign_matrix, ks_mask, sign_mask, product_mask, row_order):
    row_blocks, inner_blocks = ks_mask.shape
    col_blocks = sign_mask.shape[3]
    kept_rows = ks_matrix.astype(jnp.float32).reshape(row_blocks, BS, inner_blocks, BS)
    kept_rows = kept_rows * ks_mask.astype(jnp.float32)[:, None, :, None]
    kept_rows = kept_rows.reshape(row_blocks * BS, inner_blocks * BS)
    kept_sign = sign_matrix.astype(jnp.float32).reshape(N_ROW, N_DEPTH, KB, BS, col_blocks, BS)
    kept_sign = kept_sign * sign_mask.astype(jnp.float32)[:, :, :, None, :, None]
    kept_sign = kept_sign.reshape(N_ROW * N_DEPTH * KB * BS, col_blocks * BS)
    product = jnp.dot(kept_rows, kept_sign, precision=lax.Precision.HIGHEST, preferred_element_type=jnp.float32)
    filtered = product.reshape(row_blocks, BS, col_blocks, BS) * product_mask.astype(jnp.float32)[:, None, :, None]
    groups = row_order.shape[0]
    source_rows = (jnp.arange(groups, dtype=jnp.int32)[:, None] * MR + row_order.astype(jnp.int32)).reshape(-1)
    arranged = jnp.take(filtered, source_rows, axis=0)
    return arranged.reshape(row_blocks * BS, col_blocks * BS).astype(jnp.bfloat16)
```

```python
import jax
import jax.numpy as jnp
from jax import lax
from jax.sharding import PartitionSpec as P

BS = 128


def per_device(ks_matrix, sign_matrix, ks_mask, sign_mask, product_mask, row_order):
    row_blocks, inner_blocks = ks_mask.shape
    local_groups = sign_mask.shape[0]
    sign_inner = sign_mask.shape[2]
    col_blocks = sign_mask.shape[3]
    ks_panel = (
        ks_matrix.reshape(row_blocks, BS, inner_blocks, BS)
        * ks_mask.astype(jnp.bfloat16)[:, None, :, None]
    )
    ks_panel = ks_panel.reshape(row_blocks * BS, inner_blocks * BS)
    sign_kept = sign_matrix.reshape(local_groups, sign_inner, BS, col_blocks, BS)
    sign_kept = sign_kept * sign_mask.astype(jnp.bfloat16).reshape(
        local_groups, sign_inner, 1, col_blocks, 1
    )
    sign_kept = sign_kept.reshape(local_groups, sign_inner * BS, col_blocks * BS)
    sign_whole = lax.all_gather(sign_kept, "col", axis=0, tiled=True)
    ks_whole = lax.all_gather(ks_panel, "row", axis=0, tiled=False)
    product = jnp.einsum(
        "sik,skn->in", ks_whole, sign_whole, preferred_element_type=jnp.float32
    )
    filtered = (
        product.reshape(row_blocks, BS, col_blocks, BS)
        * product_mask.astype(jnp.float32)[:, None, :, None]
    )
    arranged = jnp.take(filtered, row_order[0], axis=0)
    arranged = arranged.reshape(row_blocks * BS, col_blocks * BS)
    summed = lax.psum_scatter(arranged, "depth", scatter_dimension=0, tiled=True)
    return summed.astype(jnp.bfloat16)


def solution(mesh):
    in_specs = (
        P("col", ("row", "depth")),
        P("col", "depth", None, "row"),
        P("col", ("row", "depth")),
        P("col", "depth", None, "row"),
        P("col", "row"),
        P("col", None),
    )
    out_specs = P(("col", "depth"), "row")
    return jax.shard_map(
        per_device, mesh=mesh, in_specs=in_specs, out_specs=out_specs, check_vma=False
    )
```

```python
import jax
import jax.numpy as jnp
from jax import lax
from jax.sharding import PartitionSpec as P

BS = 128


def swap_with(block, axis, flip):
    devices = range(lax.axis_size(axis))
    return lax.ppermute(block, axis, [(i, i ^ flip) for i in devices])


def per_device(ks_matrix, sign_matrix, ks_mask, sign_mask, product_mask, row_order):
    row_blocks, inner_blocks = ks_mask.shape
    local_groups = sign_mask.shape[0]
    sign_inner = sign_mask.shape[2]
    col_blocks = sign_mask.shape[3]
    col_count = lax.axis_size("col")
    local_order = row_order[0]
    ks_panel = (
        ks_matrix.reshape(row_blocks, BS, inner_blocks, BS)
        * ks_mask.astype(jnp.bfloat16)[:, None, :, None]
    )
    ks_panel = jnp.take(ks_panel, local_order, axis=0, mode="clip")
    ks_panel = ks_panel.reshape(row_blocks * BS, inner_blocks * BS)
    sign_kept = sign_matrix.reshape(local_groups, sign_inner, BS, col_blocks, BS)
    sign_kept = sign_kept * sign_mask.astype(jnp.bfloat16).reshape(
        local_groups, sign_inner, 1, col_blocks, 1
    )
    sign_kept = sign_kept.reshape(local_groups, sign_inner * BS, col_blocks * BS)
    far = swap_with(sign_kept, "col", 2)
    pair = jnp.concatenate([sign_kept, far], axis=0)
    near = swap_with(pair, "col", 1)
    sign_four = jnp.concatenate([pair, near], axis=0)
    me = lax.axis_index("col")
    held_cols = jnp.stack([me, me ^ 2, me ^ 1, me ^ 3])
    ks_whole = lax.all_gather(ks_panel, "row", axis=0, tiled=False)
    ks_whole = ks_whole.reshape(
        col_count, local_groups, row_blocks * BS, inner_blocks * BS
    )
    ks_matched = jnp.take(ks_whole, held_cols, axis=0, mode="clip")
    ks_matched = ks_matched.reshape(
        col_count * local_groups, row_blocks * BS, inner_blocks * BS
    )
    product = jnp.einsum(
        "sik,skn->in", ks_matched, sign_four, preferred_element_type=jnp.float32
    )
    summed = lax.psum_scatter(product, "depth", scatter_dimension=0, tiled=True)
    own_row = lax.dynamic_index_in_dim(
        local_order, lax.axis_index("depth"), 0, keepdims=False
    )
    own_mask = lax.dynamic_index_in_dim(product_mask, own_row, 0, keepdims=False)
    kept = summed.reshape(BS, col_blocks, BS) * own_mask.astype(jnp.float32)[None, :, None]
    return kept.reshape(BS, col_blocks * BS).astype(jnp.bfloat16)


def solution(mesh):
    in_specs = (
        P("col", ("row", "depth")),
        P("col", "depth", None, "row"),
        P("col", ("row", "depth")),
        P("col", "depth", None, "row"),
        P("col", "row"),
        P("col", None),
    )
    out_specs = P(("col", "depth"), "row")
    return jax.shard_map(
        per_device, mesh=mesh, in_specs=in_specs, out_specs=out_specs, check_vma=False
    )
```

```python
import jax
import jax.numpy as jnp
from jax import lax
from jax.sharding import PartitionSpec as P

BS = 128


def swap_with(block, axis, flip):
    devices = range(lax.axis_size(axis))
    return lax.ppermute(block, axis, [(i, i ^ flip) for i in devices])


def per_device(ks_matrix, sign_matrix, ks_mask, sign_mask, product_mask, row_order):
    row_blocks, inner_blocks = ks_mask.shape
    local_groups = sign_mask.shape[0]
    sign_inner = sign_mask.shape[2]
    col_blocks = sign_mask.shape[3]
    col_count = lax.axis_size("col")
    local_order = row_order[0]
    ks_panel = (
        ks_matrix.reshape(row_blocks, BS, inner_blocks, BS)
        * ks_mask.astype(jnp.bfloat16)[:, None, :, None]
    )
    ks_panel = jnp.take(ks_panel, local_order, axis=0, mode="clip")
    ks_panel = ks_panel.reshape(row_blocks * BS, inner_blocks * BS)
    sign_kept = sign_matrix.reshape(local_groups, sign_inner, BS, col_blocks, BS)
    sign_kept = sign_kept * sign_mask.astype(jnp.bfloat16).reshape(
        local_groups, sign_inner, 1, col_blocks, 1
    )
    sign_kept = sign_kept.reshape(local_groups, sign_inner * BS, col_blocks * BS)
    far = swap_with(sign_kept, "col", 2)
    pair = jnp.concatenate([sign_kept, far], axis=0)
    near = swap_with(pair, "col", 1)
    sign_four = jnp.concatenate([pair, near], axis=0)
    me = lax.axis_index("col")
    held_cols = jnp.stack([me, me ^ 2, me ^ 1, me ^ 3])
    ks_whole = lax.all_gather(ks_panel, "row", axis=0, tiled=False)
    ks_whole = ks_whole.reshape(
        col_count, local_groups, row_blocks * BS, inner_blocks * BS
    )
    ks_matched = jnp.take(ks_whole, held_cols, axis=0, mode="clip")
    ks_matched = ks_matched.reshape(
        col_count * local_groups, row_blocks * BS, inner_blocks * BS
    )
    depth_count = lax.axis_size("depth")
    pair_count = 2
    ring_count = depth_count // pair_count
    depth_me = lax.axis_index("depth")
    ring_me = depth_me // pair_count
    piece_rows = row_blocks * BS // ring_count

    def piece_for(ring_spot):
        rows = lax.dynamic_slice_in_dim(ks_matched, ring_spot * piece_rows, piece_rows, 1)
        return jnp.einsum(
            "sik,skn->in", rows, sign_four, preferred_element_type=jnp.float32
        )

    total = piece_for(ring_me)
    for shift in range(1, ring_count):
        piece = piece_for((ring_me + shift) % ring_count)
        route = [
            (d, ((d // pair_count + shift) % ring_count) * pair_count + d % pair_count)
            for d in range(depth_count)
        ]
        total = total + lax.ppermute(piece, "depth", route)
    halves = total.reshape(pair_count, BS, col_blocks * BS)
    pair_me = depth_me % pair_count
    keep = lax.dynamic_index_in_dim(halves, pair_me, 0, keepdims=False)
    give = lax.dynamic_index_in_dim(halves, 1 - pair_me, 0, keepdims=False)
    summed = keep + lax.ppermute(
        give, "depth", [(d, d ^ 1) for d in range(depth_count)]
    )
    own_row = lax.dynamic_index_in_dim(
        local_order, lax.axis_index("depth"), 0, keepdims=False
    )
    own_mask = lax.dynamic_index_in_dim(product_mask, own_row, 0, keepdims=False)
    kept = summed.reshape(BS, col_blocks, BS) * own_mask.astype(jnp.float32)[None, :, None]
    return kept.reshape(BS, col_blocks * BS).astype(jnp.bfloat16)


def solution(mesh):
    in_specs = (
        P("col", ("row", "depth")),
        P("col", "depth", None, "row"),
        P("col", ("row", "depth")),
        P("col", "depth", None, "row"),
        P("col", "row"),
        P("col", None),
    )
    out_specs = P(("col", "depth"), "row")
    return jax.shard_map(
        per_device, mesh=mesh, in_specs=in_specs, out_specs=out_specs, check_vma=False
    )
```

```python
import jax
import jax.numpy as jnp
from jax import lax
from jax.sharding import PartitionSpec as P

BS = 128


def swap_with(block, axis, flip):
    devices = range(lax.axis_size(axis))
    return lax.ppermute(block, axis, [(i, i ^ flip) for i in devices])


def per_device(ks_matrix, sign_matrix, ks_mask, sign_mask, product_mask, row_order):
    row_blocks, inner_blocks = ks_mask.shape
    local_groups = sign_mask.shape[0]
    sign_inner = sign_mask.shape[2]
    col_blocks = sign_mask.shape[3]
    col_count = lax.axis_size("col")
    depth_count = lax.axis_size("depth")
    pair_count = 2
    ring_count = depth_count // pair_count
    local_order = row_order[0]
    ks_panel = (
        ks_matrix.reshape(row_blocks, BS, inner_blocks, BS)
        * ks_mask.astype(jnp.bfloat16)[:, None, :, None]
    )
    ks_panel = jnp.take(ks_panel, local_order, axis=0, mode="clip")
    ks_halves = ks_panel.reshape(ring_count, pair_count, BS, inner_blocks * BS)
    sign_kept = sign_matrix.reshape(local_groups, sign_inner, BS, col_blocks, BS)
    sign_kept = sign_kept * sign_mask.astype(jnp.bfloat16).reshape(
        local_groups, sign_inner, 1, col_blocks, 1
    )
    sign_kept = sign_kept.reshape(local_groups, sign_inner * BS, col_blocks * BS)
    far = swap_with(sign_kept, "col", 2)
    pair = jnp.concatenate([sign_kept, far], axis=0)
    near = swap_with(pair, "col", 1)
    sign_four = jnp.concatenate([pair, near], axis=0)
    me = lax.axis_index("col")
    held_cols = jnp.stack([me, me ^ 2, me ^ 1, me ^ 3])
    depth_me = lax.axis_index("depth")
    ring_me = depth_me // pair_count
    pair_me = depth_me % pair_count

    results = []
    for owner_pair in range(pair_count):
        half = ks_halves[:, owner_pair].reshape(ring_count * BS, inner_blocks * BS)
        ks_whole = lax.all_gather(half, "row", axis=0, tiled=False)
        ks_whole = ks_whole.reshape(col_count, local_groups, ring_count * BS, inner_blocks * BS)
        ks_matched = jnp.take(ks_whole, held_cols, axis=0, mode="clip")
        ks_matched = ks_matched.reshape(
            col_count * local_groups, ring_count, BS, inner_blocks * BS
        )

        def piece_for(ring_spot):
            rows = lax.dynamic_index_in_dim(ks_matched, ring_spot, 1, keepdims=False)
            return jnp.einsum(
                "sik,skn->in", rows, sign_four, preferred_element_type=jnp.float32
            )

        total = piece_for(ring_me)
        for shift in range(1, ring_count):
            piece = piece_for((ring_me + shift) % ring_count)
            route = [
                (d, ((d // pair_count + shift) % ring_count) * pair_count + d % pair_count)
                for d in range(depth_count)
            ]
            total = total + lax.ppermute(piece, "depth", route)
        route = [(d, d ^ 1) for d in range(depth_count) if d % pair_count != owner_pair]
        results.append(total + lax.ppermute(total, "depth", route))
    summed = jnp.where(pair_me == 0, results[0], results[1])
    own_row = lax.dynamic_index_in_dim(local_order, depth_me, 0, keepdims=False)
    own_mask = lax.dynamic_index_in_dim(product_mask, own_row, 0, keepdims=False)
    kept = summed.reshape(BS, col_blocks, BS) * own_mask.astype(jnp.float32)[None, :, None]
    return kept.reshape(BS, col_blocks * BS).astype(jnp.bfloat16)


def solution(mesh):
    in_specs = (
        P("col", ("row", "depth")),
        P("col", "depth", None, "row"),
        P("col", ("row", "depth")),
        P("col", "depth", None, "row"),
        P("col", "row"),
        P("col", None),
    )
    out_specs = P(("col", "depth"), "row")
    return jax.shard_map(
        per_device, mesh=mesh, in_specs=in_specs, out_specs=out_specs, check_vma=False
    )
```

```python
import jax
import jax.numpy as jnp
from jax import lax
from jax.sharding import PartitionSpec as P

BS = 128


def swap_with(block, axis, flip):
    devices = range(lax.axis_size(axis))
    return lax.ppermute(block, axis, [(i, i ^ flip) for i in devices])


def per_device(ks_matrix, sign_matrix, ks_mask, sign_mask, product_mask, row_order):
    row_blocks, inner_blocks = ks_mask.shape
    local_groups = sign_mask.shape[0]
    sign_inner = sign_mask.shape[2]
    col_blocks = sign_mask.shape[3]
    local_order = row_order[0]
    ks_panel = (
        ks_matrix.reshape(row_blocks, BS, inner_blocks, BS)
        * ks_mask.astype(jnp.bfloat16)[:, None, :, None]
    )
    ks_panel = jnp.take(ks_panel, local_order, axis=0, mode="clip")
    ks_panel = ks_panel.reshape(row_blocks * BS, inner_blocks * BS)
    sign_kept = sign_matrix.reshape(local_groups, sign_inner, BS, col_blocks, BS)
    sign_kept = sign_kept * sign_mask.astype(jnp.bfloat16).reshape(
        local_groups, sign_inner, 1, col_blocks, 1
    )
    sign_kept = sign_kept.reshape(local_groups, sign_inner * BS, col_blocks * BS)
    far = swap_with(sign_kept, "col", 2)
    pair = jnp.concatenate([sign_kept, far], axis=0)
    near = swap_with(pair, "col", 1)
    sign_four = jnp.concatenate([pair, near], axis=0)
    row_count = lax.axis_size("row")
    row_me = lax.axis_index("row")
    rightward = [(i, (i + 1) % row_count) for i in range(row_count)]
    leftward = [(i, (i - 1) % row_count) for i in range(row_count)]
    going_right = ks_panel
    going_left = ks_panel
    panels = [ks_panel]
    offsets = [0]
    for step in range(1, row_count // 2 + 1):
        going_right = lax.ppermute(going_right, "row", rightward)
        panels.append(going_right)
        offsets.append(-step)
        if step < row_count - step:
            going_left = lax.ppermute(going_left, "row", leftward)
            panels.append(going_left)
            offsets.append(step)
    ks_matched = jnp.stack(panels)
    me = lax.axis_index("col")
    inner_of = (row_me + jnp.array(offsets, jnp.int32)) % row_count
    flipped = (inner_of // local_groups) ^ me
    spot = (flipped % 2) * 2 + flipped // 2
    sign_four = jnp.take(sign_four, spot * local_groups + inner_of % local_groups, axis=0, mode="clip")
    depth_count = lax.axis_size("depth")
    pair_count = 2
    ring_count = depth_count // pair_count
    depth_me = lax.axis_index("depth")
    ring_me = depth_me // pair_count
    piece_rows = row_blocks * BS // ring_count

    def piece_for(ring_spot):
        rows = lax.dynamic_slice_in_dim(ks_matched, ring_spot * piece_rows, piece_rows, 1)
        return jnp.einsum(
            "sik,skn->in", rows, sign_four, preferred_element_type=jnp.float32
        )

    total = piece_for(ring_me)
    for shift in range(1, ring_count):
        piece = piece_for((ring_me + shift) % ring_count)
        route = [
            (d, ((d // pair_count + shift) % ring_count) * pair_count + d % pair_count)
            for d in range(depth_count)
        ]
        total = total + lax.ppermute(piece, "depth", route)
    halves = total.reshape(pair_count, BS, col_blocks * BS)
    pair_me = depth_me % pair_count
    keep = lax.dynamic_index_in_dim(halves, pair_me, 0, keepdims=False)
    give = lax.dynamic_index_in_dim(halves, 1 - pair_me, 0, keepdims=False)
    summed = keep + lax.ppermute(
        give, "depth", [(d, d ^ 1) for d in range(depth_count)]
    )
    own_row = lax.dynamic_index_in_dim(
        local_order, lax.axis_index("depth"), 0, keepdims=False
    )
    own_mask = lax.dynamic_index_in_dim(product_mask, own_row, 0, keepdims=False)
    kept = summed.reshape(BS, col_blocks, BS) * own_mask.astype(jnp.float32)[None, :, None]
    return kept.reshape(BS, col_blocks * BS).astype(jnp.bfloat16)


def solution(mesh):
    in_specs = (
        P("col", ("row", "depth")),
        P("col", "depth", None, "row"),
        P("col", ("row", "depth")),
        P("col", "depth", None, "row"),
        P("col", "row"),
        P("col", None),
    )
    out_specs = P(("col", "depth"), "row")
    return jax.shard_map(
        per_device, mesh=mesh, in_specs=in_specs, out_specs=out_specs, check_vma=False
    )
```

```python
import jax
import jax.numpy as jnp
from jax import lax
from jax.sharding import PartitionSpec as P

BS = 128


def swap_with(block, axis, flip):
    devices = range(lax.axis_size(axis))
    return lax.ppermute(block, axis, [(i, i ^ flip) for i in devices])


def per_device(ks_matrix, sign_matrix, ks_mask, sign_mask, product_mask, row_order):
    row_blocks, inner_blocks = ks_mask.shape
    local_groups = sign_mask.shape[0]
    sign_inner = sign_mask.shape[2]
    col_blocks = sign_mask.shape[3]
    local_order = row_order[0]
    ks_panel = (
        ks_matrix.reshape(row_blocks, BS, inner_blocks, BS)
        * ks_mask.astype(jnp.bfloat16)[:, None, :, None]
    )
    ks_panel = jnp.take(ks_panel, local_order, axis=0, mode="clip")
    ks_panel = ks_panel.reshape(row_blocks * BS, inner_blocks * BS)
    sign_kept = sign_matrix.reshape(local_groups, sign_inner, BS, col_blocks, BS)
    sign_kept = sign_kept * sign_mask.astype(jnp.bfloat16).reshape(
        local_groups, sign_inner, 1, col_blocks, 1
    )
    sign_kept = sign_kept.reshape(local_groups, sign_inner * BS, col_blocks * BS)
    far = swap_with(sign_kept, "col", 2)
    pair = jnp.concatenate([sign_kept, far], axis=0)
    near = swap_with(pair, "col", 1)
    sign_four = jnp.concatenate([pair, near], axis=0)
    me = lax.axis_index("col")
    ks_whole = lax.all_gather(ks_panel, "row", axis=0, tiled=False)
    inner_of = jnp.arange(lax.axis_size("row"), dtype=jnp.int32)
    flipped = (inner_of // local_groups) ^ me
    spot = (flipped % 2) * 2 + flipped // 2
    sign_four = jnp.take(sign_four, spot * local_groups + inner_of % local_groups, axis=0, mode="clip")
    product = jnp.einsum(
        "sik,skn->in", ks_whole, sign_four, preferred_element_type=jnp.float32
    )
    parts = product.reshape(row_blocks, BS, col_blocks * BS)
    arrived = lax.all_to_all(parts, "depth", 0, 0, tiled=True)
    summed = jnp.sum(arrived, axis=0)
    own_row = lax.dynamic_index_in_dim(
        local_order, lax.axis_index("depth"), 0, keepdims=False
    )
    own_mask = lax.dynamic_index_in_dim(product_mask, own_row, 0, keepdims=False)
    kept = summed.reshape(BS, col_blocks, BS) * own_mask.astype(jnp.float32)[None, :, None]
    return kept.reshape(BS, col_blocks * BS).astype(jnp.bfloat16)


def solution(mesh):
    in_specs = (
        P("col", ("row", "depth")),
        P("col", "depth", None, "row"),
        P("col", ("row", "depth")),
        P("col", "depth", None, "row"),
        P("col", "row"),
        P("col", None),
    )
    out_specs = P(("col", "depth"), "row")
    return jax.shard_map(
        per_device, mesh=mesh, in_specs=in_specs, out_specs=out_specs, check_vma=False
    )
```

```python
import jax
import jax.numpy as jnp
from jax import lax
from jax.sharding import PartitionSpec as P

BS = 128


def swap_with(block, axis, flip):
    devices = range(lax.axis_size(axis))
    return lax.ppermute(block, axis, [(i, i ^ flip) for i in devices])


def per_device(ks_matrix, sign_matrix, ks_mask, sign_mask, product_mask, row_order):
    row_blocks, inner_blocks = ks_mask.shape
    local_groups = sign_mask.shape[0]
    sign_inner = sign_mask.shape[2]
    col_blocks = sign_mask.shape[3]
    local_order = row_order[0]
    ks_panel = (
        ks_matrix.reshape(row_blocks, BS, inner_blocks, BS)
        * ks_mask.astype(jnp.bfloat16)[:, None, :, None]
    )
    ks_panel = jnp.take(ks_panel, local_order, axis=0, mode="clip")
    ks_panel = ks_panel.reshape(row_blocks * BS, inner_blocks * BS)
    sign_kept = sign_matrix.reshape(local_groups, sign_inner, BS, col_blocks, BS)
    sign_kept = sign_kept * sign_mask.astype(jnp.bfloat16).reshape(
        local_groups, sign_inner, 1, col_blocks, 1
    )
    sign_kept = sign_kept.reshape(local_groups, sign_inner * BS, col_blocks * BS)
    far = swap_with(sign_kept, "col", 2)
    pair = jnp.concatenate([sign_kept, far], axis=0)
    near = swap_with(pair, "col", 1)
    sign_four = jnp.concatenate([pair, near], axis=0)
    me = lax.axis_index("col")
    row_count = lax.axis_size("row")
    row_me = lax.axis_index("row")
    half_rows = BS // 2
    split = ks_panel.reshape(row_blocks, 2, half_rows, inner_blocks * BS)
    low = split[:, 0].reshape(row_blocks * half_rows, inner_blocks * BS)
    high = split[:, 1].reshape(row_blocks * half_rows, inner_blocks * BS)

    def sign_in_order(inner_of):
        flipped = (inner_of // local_groups) ^ me
        spot = (flipped % 2) * 2 + flipped // 2
        return jnp.take(sign_four, spot * local_groups + inner_of % local_groups, axis=0, mode="clip")

    def reduced_over_depth(panels, signs):
        product = jnp.einsum(
            "sik,skn->in", panels, signs, preferred_element_type=jnp.float32
        )
        parts = product.reshape(row_blocks, half_rows, col_blocks * BS)
        arrived = lax.all_to_all(parts, "depth", 0, 0, tiled=True)
        return jnp.sum(arrived, axis=0)

    low_whole = lax.all_gather(low, "row", axis=0, tiled=False)
    rightward = [(i, (i + 1) % row_count) for i in range(row_count)]
    leftward = [(i, (i - 1) % row_count) for i in range(row_count)]
    going_right = high
    going_left = high
    panels = [high]
    offsets = [0]
    for step in range(1, row_count // 2 + 1):
        going_right = lax.ppermute(going_right, "row", rightward)
        panels.append(going_right)
        offsets.append(-step)
        if step < row_count - step:
            going_left = lax.ppermute(going_left, "row", leftward)
            panels.append(going_left)
            offsets.append(step)
    ring_inner = (row_me + jnp.array(offsets, jnp.int32)) % row_count
    high_sum = reduced_over_depth(jnp.stack(panels), sign_in_order(ring_inner))
    low_sum = reduced_over_depth(
        low_whole, sign_in_order(jnp.arange(row_count, dtype=jnp.int32))
    )
    summed = jnp.concatenate([low_sum, high_sum], axis=0)
    own_row = lax.dynamic_index_in_dim(
        local_order, lax.axis_index("depth"), 0, keepdims=False
    )
    own_mask = lax.dynamic_index_in_dim(product_mask, own_row, 0, keepdims=False)
    kept = summed.reshape(BS, col_blocks, BS) * own_mask.astype(jnp.float32)[None, :, None]
    return kept.reshape(BS, col_blocks * BS).astype(jnp.bfloat16)


def solution(mesh):
    in_specs = (
        P("col", ("row", "depth")),
        P("col", "depth", None, "row"),
        P("col", ("row", "depth")),
        P("col", "depth", None, "row"),
        P("col", "row"),
        P("col", None),
    )
    out_specs = P(("col", "depth"), "row")
    return jax.shard_map(
        per_device, mesh=mesh, in_specs=in_specs, out_specs=out_specs, check_vma=False
    )
```

```python
import jax
import jax.numpy as jnp
from jax import lax
from jax.sharding import Mesh, PartitionSpec as P

BS = 128


def swap_with(block, axis, flip):
    devices = range(lax.axis_size(axis))
    return lax.ppermute(block, axis, [(i, i ^ flip) for i in devices])


def per_device(ks_matrix, sign_matrix, ks_mask, sign_mask, product_mask, row_order):
    row_blocks, inner_blocks = ks_mask.shape
    local_groups = sign_mask.shape[0]
    sign_inner = sign_mask.shape[2]
    col_blocks = sign_mask.shape[3]
    local_order = row_order[0]
    ks_panel = (
        ks_matrix.reshape(row_blocks, BS, inner_blocks, BS)
        * ks_mask.astype(jnp.bfloat16)[:, None, :, None]
    )
    ks_panel = jnp.take(ks_panel, local_order, axis=0, mode="clip")
    ks_panel = ks_panel.reshape(row_blocks * BS, inner_blocks * BS)
    sign_kept = sign_matrix.reshape(local_groups, sign_inner, BS, col_blocks, BS)
    sign_kept = sign_kept * sign_mask.astype(jnp.bfloat16).reshape(
        local_groups, sign_inner, 1, col_blocks, 1
    )
    sign_kept = sign_kept.reshape(local_groups, sign_inner * BS, col_blocks * BS)
    far = swap_with(sign_kept, "col", 2)
    pair = jnp.concatenate([sign_kept, far], axis=0)
    near = swap_with(pair, "col", 1)
    sign_four = jnp.concatenate([pair, near], axis=0)
    me = lax.axis_index("col")
    near_count = lax.axis_size("near")
    far_count = lax.axis_size("far")
    ks_whole = lax.all_gather(ks_panel, "far", axis=0, tiled=False)
    ks_whole = lax.all_gather(ks_whole, "near", axis=0, tiled=True)
    spots = jnp.arange(near_count * far_count, dtype=jnp.int32)
    inner_of = (spots % far_count) * near_count + spots // far_count
    flipped = (inner_of // local_groups) ^ me
    spot = (flipped % 2) * 2 + flipped // 2
    sign_four = jnp.take(sign_four, spot * local_groups + inner_of % local_groups, axis=0, mode="clip")
    product = jnp.einsum(
        "sik,skn->in", ks_whole, sign_four, preferred_element_type=jnp.float32
    )
    parts = product.reshape(row_blocks, BS, col_blocks * BS)
    arrived = lax.all_to_all(parts, "depth", 0, 0, tiled=True)
    summed = jnp.sum(arrived, axis=0)
    own_row = lax.dynamic_index_in_dim(
        local_order, lax.axis_index("depth"), 0, keepdims=False
    )
    own_mask = lax.dynamic_index_in_dim(product_mask, own_row, 0, keepdims=False)
    kept = summed.reshape(BS, col_blocks, BS) * own_mask.astype(jnp.float32)[None, :, None]
    return kept.reshape(BS, col_blocks * BS).astype(jnp.bfloat16)


def solution(mesh):
    rows, cols, depths = mesh.devices.shape
    near_count = 2
    split_mesh = Mesh(
        mesh.devices.reshape(rows // near_count, near_count, cols, depths),
        ("far", "near", "col", "depth"),
    )
    row = ("far", "near")
    in_specs = (
        P("col", (*row, "depth")),
        P("col", "depth", None, row),
        P("col", (*row, "depth")),
        P("col", "depth", None, row),
        P("col", row),
        P("col", None),
    )
    out_specs = P(("col", "depth"), row)
    return jax.shard_map(
        per_device, mesh=split_mesh, in_specs=in_specs, out_specs=out_specs, check_vma=False
    )
```

```python
import jax
import jax.numpy as jnp
from jax import lax
from jax.sharding import PartitionSpec as P

BS = 128


def swap_with(block, axis, flip):
    devices = range(lax.axis_size(axis))
    return lax.ppermute(block, axis, [(i, i ^ flip) for i in devices])


def per_device(ks_matrix, sign_matrix, ks_mask, sign_mask, product_mask, row_order):
    row_blocks, inner_blocks = ks_mask.shape
    local_groups = sign_mask.shape[0]
    sign_inner = sign_mask.shape[2]
    col_blocks = sign_mask.shape[3]
    local_order = row_order[0]
    ks_blocks = ks_matrix.reshape(row_blocks, BS, inner_blocks, BS)
    ks_blocks = jnp.take(ks_blocks, local_order, axis=0, mode="clip")
    row_mask = jnp.take(ks_mask, local_order, axis=0, mode="clip")
    ks_panel = ks_blocks * row_mask.astype(jnp.bfloat16)[:, None, :, None]
    ks_panel = ks_panel.reshape(row_blocks * BS, inner_blocks * BS)
    sign_kept = sign_matrix.reshape(local_groups, sign_inner, BS, col_blocks, BS)
    sign_kept = sign_kept * sign_mask.astype(jnp.bfloat16).reshape(
        local_groups, sign_inner, 1, col_blocks, 1
    )
    sign_kept = sign_kept.reshape(local_groups, sign_inner * BS, col_blocks * BS)
    far = swap_with(sign_kept, "col", 2)
    pair = jnp.concatenate([sign_kept, far], axis=0)
    near = swap_with(pair, "col", 1)
    sign_four = jnp.concatenate([pair, near], axis=0)
    me = lax.axis_index("col")
    ks_whole = lax.all_gather(ks_panel, "row", axis=0, tiled=False)
    inner_of = jnp.arange(lax.axis_size("row"), dtype=jnp.int32)
    flipped = (inner_of // local_groups) ^ me
    spot = (flipped % 2) * 2 + flipped // 2
    sign_four = jnp.take(sign_four, spot * local_groups + inner_of % local_groups, axis=0, mode="clip")
    halves = []
    half_cols = col_blocks * BS // 2
    for half in range(2):
        product = jnp.einsum(
            "sik,skn->in",
            ks_whole,
            sign_four[:, :, half * half_cols:(half + 1) * half_cols],
            preferred_element_type=jnp.float32,
        )
        parts = product.reshape(row_blocks, BS, half_cols)
        arrived = lax.all_to_all(parts, "depth", 0, 0, tiled=True)
        halves.append(jnp.sum(arrived, axis=0))
    summed = jnp.concatenate(halves, axis=1)
    own_row = lax.dynamic_index_in_dim(
        local_order, lax.axis_index("depth"), 0, keepdims=False
    )
    own_mask = lax.dynamic_index_in_dim(product_mask, own_row, 0, keepdims=False)
    kept = summed.reshape(BS, col_blocks, BS) * own_mask.astype(jnp.float32)[None, :, None]
    return kept.reshape(BS, col_blocks * BS).astype(jnp.bfloat16)


def solution(mesh):
    in_specs = (
        P("col", ("row", "depth")),
        P("col", "depth", None, "row"),
        P("col", ("row", "depth")),
        P("col", "depth", None, "row"),
        P("col", "row"),
        P("col", None),
    )
    out_specs = P(("col", "depth"), "row")
    return jax.shard_map(
        per_device, mesh=mesh, in_specs=in_specs, out_specs=out_specs, check_vma=False
    )
```

```python
import jax
import jax.numpy as jnp
from jax import lax
from jax.sharding import PartitionSpec as P

BS = 128


def swap_with(block, axis, flip):
    devices = range(lax.axis_size(axis))
    return lax.ppermute(block, axis, [(i, i ^ flip) for i in devices])


def per_device(ks_matrix, sign_matrix, ks_mask, sign_mask, product_mask, row_order):
    row_blocks, inner_blocks = ks_mask.shape
    local_groups = sign_mask.shape[0]
    sign_inner = sign_mask.shape[2]
    col_blocks = sign_mask.shape[3]
    local_order = row_order[0]
    ks_panel = (
        ks_matrix.reshape(row_blocks, BS, inner_blocks, BS)
        * ks_mask.astype(jnp.bfloat16)[:, None, :, None]
    )
    ks_panel = jnp.take(ks_panel, local_order, axis=0, mode="clip")
    ks_panel = ks_panel.reshape(row_blocks * BS, inner_blocks * BS)
    sign_kept = sign_matrix.reshape(local_groups, sign_inner, BS, col_blocks, BS)
    sign_kept = sign_kept * sign_mask.astype(jnp.bfloat16).reshape(
        local_groups, sign_inner, 1, col_blocks, 1
    )
    sign_kept = sign_kept.reshape(local_groups, sign_inner * BS, col_blocks * BS)
    far = swap_with(sign_kept, "col", 2)
    pair = jnp.concatenate([sign_kept, far], axis=0)
    near = swap_with(pair, "col", 1)
    sign_four = jnp.concatenate([pair, near], axis=0)
    me = lax.axis_index("col")
    ks_whole = lax.all_gather(ks_panel, "row", axis=1, tiled=True)
    inner_of = jnp.arange(lax.axis_size("row"), dtype=jnp.int32)
    flipped = (inner_of // local_groups) ^ me
    spot = (flipped % 2) * 2 + flipped // 2
    sign_four = jnp.take(sign_four, spot * local_groups + inner_of % local_groups, axis=0, mode="clip")
    product = jnp.dot(
        ks_whole,
        sign_four.reshape(-1, col_blocks * BS),
        preferred_element_type=jnp.float32,
    )
    parts = product.reshape(row_blocks, BS, col_blocks * BS)
    arrived = lax.all_to_all(parts, "depth", 0, 0, tiled=True)
    summed = jnp.sum(arrived, axis=0)
    own_row = lax.dynamic_index_in_dim(
        local_order, lax.axis_index("depth"), 0, keepdims=False
    )
    own_mask = lax.dynamic_index_in_dim(product_mask, own_row, 0, keepdims=False)
    kept = summed.reshape(BS, col_blocks, BS) * own_mask.astype(jnp.float32)[None, :, None]
    return kept.reshape(BS, col_blocks * BS).astype(jnp.bfloat16)


def solution(mesh):
    in_specs = (
        P("col", ("row", "depth")),
        P("col", "depth", None, "row"),
        P("col", ("row", "depth")),
        P("col", "depth", None, "row"),
        P("col", "row"),
        P("col", None),
    )
    out_specs = P(("col", "depth"), "row")
    return jax.shard_map(
        per_device, mesh=mesh, in_specs=in_specs, out_specs=out_specs, check_vma=False
    )
```

```python
import jax
import jax.numpy as jnp
from jax import lax
from jax.sharding import Mesh, PartitionSpec as P

BS = 128


def swap_with(block, axis, flip):
    devices = range(lax.axis_size(axis))
    return lax.ppermute(block, axis, [(i, i ^ flip) for i in devices])


def per_device(ks_matrix, sign_matrix, ks_mask, sign_mask, product_mask, row_order):
    row_blocks, inner_blocks = ks_mask.shape
    local_groups = sign_mask.shape[0]
    sign_inner = sign_mask.shape[2]
    col_blocks = sign_mask.shape[3]
    ring_count = lax.axis_size("y")
    pair_count = lax.axis_size("xlo")
    ring_me = lax.axis_index("y")
    pair_me = lax.axis_index("xlo")
    local_order = row_order[0]
    ks_panel = (
        ks_matrix.reshape(row_blocks, BS, inner_blocks, BS)
        * ks_mask.astype(jnp.bfloat16)[:, None, :, None]
    )
    ks_panel = jnp.take(ks_panel, local_order, axis=0, mode="clip")
    ks_split = ks_panel.reshape(ring_count, pair_count, BS, inner_blocks * BS)
    mine = lax.dynamic_index_in_dim(ks_split, pair_me, 1, keepdims=False)
    theirs = lax.dynamic_index_in_dim(ks_split, 1 - pair_me, 1, keepdims=False)
    lent = swap_with(theirs, "xlo", 1)
    payload = jnp.stack([mine, lent])
    payload = payload.reshape(pair_count, ring_count * BS, inner_blocks * BS)
    sign_kept = sign_matrix.reshape(local_groups, sign_inner, BS, col_blocks, BS)
    sign_kept = sign_kept * sign_mask.astype(jnp.bfloat16).reshape(
        local_groups, sign_inner, 1, col_blocks, 1
    )
    sign_kept = sign_kept.reshape(local_groups, sign_inner * BS, col_blocks * BS)
    sign_kept = jnp.stack([sign_kept, swap_with(sign_kept, "xlo", 1)])
    far = swap_with(sign_kept, "col", 2)
    pair = jnp.concatenate([sign_kept, far], axis=1)
    near = swap_with(pair, "col", 1)
    sign_four = jnp.concatenate([pair, near], axis=1)
    me = lax.axis_index("col")
    ks_whole = lax.all_gather(payload, "row", axis=0, tiled=False)
    inner_of = jnp.arange(lax.axis_size("row"), dtype=jnp.int32)
    flipped = (inner_of // local_groups) ^ me
    spot = (flipped % 2) * 2 + flipped // 2
    sign_four = jnp.take(sign_four, spot * local_groups + inner_of % local_groups, axis=1, mode="clip")
    product = jnp.einsum(
        "sjik,jskn->in", ks_whole, sign_four, preferred_element_type=jnp.float32
    )
    parts = product.reshape(ring_count, BS, col_blocks * BS)
    arrived = lax.all_to_all(parts, "y", 0, 0, tiled=True)
    summed = jnp.sum(arrived, axis=0)
    own_row = lax.dynamic_index_in_dim(
        local_order, ring_me * pair_count + pair_me, 0, keepdims=False
    )
    own_mask = lax.dynamic_index_in_dim(product_mask, own_row, 0, keepdims=False)
    kept = summed.reshape(BS, col_blocks, BS) * own_mask.astype(jnp.float32)[None, :, None]
    return kept.reshape(BS, col_blocks * BS).astype(jnp.bfloat16)


def solution(mesh):
    rows, cols, depths = mesh.devices.shape
    pair_count = 2
    split_mesh = Mesh(
        mesh.devices.reshape(rows, cols, depths // pair_count, pair_count),
        ("row", "col", "y", "xlo"),
    )
    depth = ("y", "xlo")
    in_specs = (
        P("col", ("row", *depth)),
        P("col", depth, None, "row"),
        P("col", ("row", *depth)),
        P("col", depth, None, "row"),
        P("col", "row"),
        P("col", None),
    )
    out_specs = P(("col", *depth), "row")
    return jax.shard_map(
        per_device, mesh=split_mesh, in_specs=in_specs, out_specs=out_specs, check_vma=False
    )
```

```python
import jax
import jax.numpy as jnp
from jax import lax
from jax.sharding import Mesh, PartitionSpec as P

BS = 128


def swap_with(block, axis, flip):
    devices = range(lax.axis_size(axis))
    return lax.ppermute(block, axis, [(i, i ^ flip) for i in devices])


def per_device(ks_matrix, sign_matrix, ks_mask, sign_mask, product_mask, row_order):
    row_blocks, inner_blocks = ks_mask.shape
    local_groups = sign_mask.shape[0]
    sign_inner = sign_mask.shape[2]
    col_blocks = sign_mask.shape[3]
    ring_count = lax.axis_size("y")
    pair_count = lax.axis_size("xlo")
    ring_me = lax.axis_index("y")
    pair_me = lax.axis_index("xlo")
    local_order = row_order[0]
    ks_blocks = ks_matrix.reshape(row_blocks, BS, inner_blocks, BS)
    by_pair = local_order.reshape(ring_count, pair_count)

    def arranged_rows(pair):
        picked = lax.dynamic_index_in_dim(by_pair, pair, 1, keepdims=False)
        rows = jnp.take(ks_blocks, picked, axis=0, mode="clip")
        row_mask = jnp.take(ks_mask, picked, axis=0, mode="clip")
        rows = rows * row_mask.astype(jnp.bfloat16)[:, None, :, None]
        return rows.reshape(ring_count, BS, inner_blocks * BS)

    lent = swap_with(arranged_rows(1 - pair_me), "xlo", 1)
    mine = arranged_rows(pair_me)
    payload = jnp.stack([mine, lent])
    payload = payload.reshape(pair_count, ring_count * BS, inner_blocks * BS)
    sign_kept = sign_matrix.reshape(local_groups, sign_inner, BS, col_blocks, BS)
    sign_kept = sign_kept * sign_mask.astype(jnp.bfloat16).reshape(
        local_groups, sign_inner, 1, col_blocks, 1
    )
    sign_kept = sign_kept.reshape(local_groups, sign_inner * BS, col_blocks * BS)
    sign_kept = jnp.stack([sign_kept, swap_with(sign_kept, "xlo", 1)])
    far = swap_with(sign_kept, "col", 2)
    pair = jnp.concatenate([sign_kept, far], axis=1)
    near = swap_with(pair, "col", 1)
    sign_four = jnp.concatenate([pair, near], axis=1)
    me = lax.axis_index("col")
    ks_whole = lax.all_gather(payload, "row", axis=0, tiled=False)
    inner_of = jnp.arange(lax.axis_size("row"), dtype=jnp.int32)
    flipped = (inner_of // local_groups) ^ me
    spot = (flipped % 2) * 2 + flipped // 2
    sign_four = jnp.take(sign_four, spot * local_groups + inner_of % local_groups, axis=1, mode="clip")
    product = jnp.einsum(
        "sjik,jskn->in", ks_whole, sign_four, preferred_element_type=jnp.float32
    )
    parts = product.reshape(ring_count, BS, col_blocks * BS)
    arrived = lax.all_to_all(parts, "y", 0, 0, tiled=True)
    summed = jnp.sum(arrived, axis=0)
    own_row = lax.dynamic_index_in_dim(
        local_order, ring_me * pair_count + pair_me, 0, keepdims=False
    )
    own_mask = lax.dynamic_index_in_dim(product_mask, own_row, 0, keepdims=False)
    kept = summed.reshape(BS, col_blocks, BS) * own_mask.astype(jnp.float32)[None, :, None]
    return kept.reshape(BS, col_blocks * BS).astype(jnp.bfloat16)


def solution(mesh):
    rows, cols, depths = mesh.devices.shape
    pair_count = 2
    split_mesh = Mesh(
        mesh.devices.reshape(rows, cols, depths // pair_count, pair_count),
        ("row", "col", "y", "xlo"),
    )
    depth = ("y", "xlo")
    in_specs = (
        P("col", ("row", *depth)),
        P("col", depth, None, "row"),
        P("col", ("row", *depth)),
        P("col", depth, None, "row"),
        P("col", "row"),
        P("col", None),
    )
    out_specs = P(("col", *depth), "row")
    return jax.shard_map(
        per_device, mesh=split_mesh, in_specs=in_specs, out_specs=out_specs, check_vma=False
    )
```

```python
import jax
import jax.numpy as jnp
from jax import lax
from jax.sharding import Mesh, PartitionSpec as P

BS = 128


def swap_with(block, axis, flip):
    devices = range(lax.axis_size(axis))
    return lax.ppermute(block, axis, [(i, i ^ flip) for i in devices])


def per_device(ks_matrix, sign_matrix, ks_mask, sign_mask, product_mask, row_order):
    row_blocks, inner_blocks = ks_mask.shape
    local_groups = sign_mask.shape[0]
    sign_inner = sign_mask.shape[2]
    col_blocks = sign_mask.shape[3]
    ring_count = lax.axis_size("y")
    pair_count = lax.axis_size("xlo")
    ring_me = lax.axis_index("y")
    pair_me = lax.axis_index("xlo")
    local_order = row_order[0]
    ks_panel = (
        ks_matrix.reshape(row_blocks, BS, inner_blocks, BS)
        * ks_mask.astype(jnp.bfloat16)[:, None, :, None]
    )
    ks_panel = jnp.take(ks_panel, local_order, axis=0, mode="clip")
    ks_split = ks_panel.reshape(ring_count, pair_count, BS, inner_blocks * BS)
    mine = lax.dynamic_index_in_dim(ks_split, pair_me, 1, keepdims=False)
    theirs = lax.dynamic_index_in_dim(ks_split, 1 - pair_me, 1, keepdims=False)
    lent = swap_with(theirs, "xlo", 1)
    payload = jnp.stack([mine, lent])
    payload = payload.reshape(pair_count, ring_count * BS, inner_blocks * BS)
    sign_kept = sign_matrix.reshape(local_groups, sign_inner, BS, col_blocks, BS)
    sign_kept = sign_kept * sign_mask.astype(jnp.bfloat16).reshape(
        local_groups, sign_inner, 1, col_blocks, 1
    )
    sign_kept = sign_kept.reshape(local_groups, sign_inner * BS, col_blocks * BS)
    sign_kept = jnp.stack([sign_kept, swap_with(sign_kept, "xlo", 1)])
    me = lax.axis_index("col")
    chip_bit = me // 2
    core_bit = me % 2
    far = swap_with(sign_kept, "col", 2)
    pair = jnp.where(
        chip_bit == 0,
        jnp.concatenate([sign_kept, far], axis=1),
        jnp.concatenate([far, sign_kept], axis=1),
    )
    near = swap_with(pair, "col", 1)
    core0 = jnp.where(core_bit == 0, pair, near)
    core1 = jnp.where(core_bit == 0, near, pair)
    shape = (pair_count, 2, local_groups, sign_inner * BS, col_blocks * BS)
    sign_four = jnp.stack([core0.reshape(shape), core1.reshape(shape)], axis=2)
    sign_four = sign_four.reshape(pair_count, -1, sign_inner * BS, col_blocks * BS)
    ks_whole = lax.all_gather(payload, "row", axis=0, tiled=False)
    product = jnp.einsum(
        "sjik,jskn->in", ks_whole, sign_four, preferred_element_type=jnp.float32
    )
    parts = product.reshape(ring_count, BS, col_blocks * BS)
    arrived = lax.all_to_all(parts, "y", 0, 0, tiled=True)
    summed = jnp.sum(arrived, axis=0)
    own_row = lax.dynamic_index_in_dim(
        local_order, ring_me * pair_count + pair_me, 0, keepdims=False
    )
    own_mask = lax.dynamic_index_in_dim(product_mask, own_row, 0, keepdims=False)
    kept = summed.reshape(BS, col_blocks, BS) * own_mask.astype(jnp.float32)[None, :, None]
    return kept.reshape(BS, col_blocks * BS).astype(jnp.bfloat16)


def solution(mesh):
    rows, cols, depths = mesh.devices.shape
    pair_count = 2
    split_mesh = Mesh(
        mesh.devices.reshape(rows, cols, depths // pair_count, pair_count),
        ("row", "col", "y", "xlo"),
    )
    depth = ("y", "xlo")
    in_specs = (
        P("col", ("row", *depth)),
        P("col", depth, None, "row"),
        P("col", ("row", *depth)),
        P("col", depth, None, "row"),
        P("col", "row"),
        P("col", None),
    )
    out_specs = P(("col", *depth), "row")
    return jax.shard_map(
        per_device, mesh=split_mesh, in_specs=in_specs, out_specs=out_specs, check_vma=False
    )
```

```python
import jax
import jax.numpy as jnp
from jax import lax
from jax.sharding import Mesh, PartitionSpec as P

BS = 128


def swap_with(block, axis, flip):
    devices = range(lax.axis_size(axis))
    return lax.ppermute(block, axis, [(i, i ^ flip) for i in devices])


def per_device(ks_matrix, sign_matrix, ks_mask, sign_mask, product_mask, row_order):
    row_blocks, inner_blocks = ks_mask.shape
    local_groups = sign_mask.shape[0]
    sign_inner = sign_mask.shape[2]
    col_blocks = sign_mask.shape[3]
    ring_count = lax.axis_size("y")
    pair_count = lax.axis_size("xlo")
    ring_me = lax.axis_index("y")
    pair_me = lax.axis_index("xlo")
    local_order = row_order[0]
    ks_panel = (
        ks_matrix.reshape(row_blocks, BS, inner_blocks, BS)
        * ks_mask.astype(jnp.bfloat16)[:, None, :, None]
    )
    ks_panel = jnp.take(ks_panel, local_order, axis=0, mode="clip")
    ks_split = ks_panel.reshape(ring_count, pair_count, BS, inner_blocks * BS)
    mine = lax.dynamic_index_in_dim(ks_split, pair_me, 1, keepdims=False)
    theirs = lax.dynamic_index_in_dim(ks_split, 1 - pair_me, 1, keepdims=False)
    lent = swap_with(theirs, "xlo", 1)
    payload = jnp.stack([mine, lent])
    payload = payload.reshape(pair_count, ring_count * BS, inner_blocks * BS)
    sign_kept = sign_matrix.reshape(local_groups, sign_inner, BS, col_blocks, BS)
    sign_kept = sign_kept * sign_mask.astype(jnp.bfloat16).reshape(
        local_groups, sign_inner, 1, col_blocks, 1
    )
    sign_kept = sign_kept.reshape(local_groups, sign_inner * BS, col_blocks * BS)
    me = lax.axis_index("col")
    chip_bit = me // 2
    core_bit = me % 2
    partner = swap_with(sign_kept, "xlo", 1)
    diag = swap_with(sign_kept, ("col", "xlo"), 5)
    far = swap_with(diag, "xlo", 1)
    mine_first = jnp.stack(
        [jnp.concatenate([sign_kept, far]), jnp.concatenate([partner, diag])]
    )
    far_first = jnp.stack(
        [jnp.concatenate([far, sign_kept]), jnp.concatenate([diag, partner])]
    )
    pair = jnp.where(chip_bit == 0, mine_first, far_first)
    near = swap_with(pair, "col", 1)
    core0 = jnp.where(core_bit == 0, pair, near)
    core1 = jnp.where(core_bit == 0, near, pair)
    shape = (pair_count, 2, local_groups, sign_inner * BS, col_blocks * BS)
    sign_four = jnp.stack([core0.reshape(shape), core1.reshape(shape)], axis=2)
    sign_four = sign_four.reshape(pair_count, -1, sign_inner * BS, col_blocks * BS)
    ks_whole = lax.all_gather(payload, "row", axis=0, tiled=False)
    product = jnp.einsum(
        "sjik,jskn->in", ks_whole, sign_four, preferred_element_type=jnp.float32
    )
    parts = product.reshape(ring_count, BS, col_blocks * BS)
    arrived = lax.all_to_all(parts, "y", 0, 0, tiled=True)
    summed = jnp.sum(arrived, axis=0)
    own_row = lax.dynamic_index_in_dim(
        local_order, ring_me * pair_count + pair_me, 0, keepdims=False
    )
    own_mask = lax.dynamic_index_in_dim(product_mask, own_row, 0, keepdims=False)
    kept = summed.reshape(BS, col_blocks, BS) * own_mask.astype(jnp.float32)[None, :, None]
    return kept.reshape(BS, col_blocks * BS).astype(jnp.bfloat16)


def solution(mesh):
    rows, cols, depths = mesh.devices.shape
    pair_count = 2
    split_mesh = Mesh(
        mesh.devices.reshape(rows, cols, depths // pair_count, pair_count),
        ("row", "col", "y", "xlo"),
    )
    depth = ("y", "xlo")
    in_specs = (
        P("col", ("row", *depth)),
        P("col", depth, None, "row"),
        P("col", ("row", *depth)),
        P("col", depth, None, "row"),
        P("col", "row"),
        P("col", None),
    )
    out_specs = P(("col", *depth), "row")
    return jax.shard_map(
        per_device, mesh=split_mesh, in_specs=in_specs, out_specs=out_specs, check_vma=False
    )
```

```python
import jax
import jax.numpy as jnp
from jax import lax
from jax.sharding import Mesh, PartitionSpec as P

BS = 128


def swap_with(block, axis, flip):
    devices = range(lax.axis_size(axis))
    return lax.ppermute(block, axis, [(i, i ^ flip) for i in devices])


def per_device(ks_matrix, sign_matrix, ks_mask, sign_mask, product_mask, row_order):
    row_blocks, inner_blocks = ks_mask.shape
    local_groups = sign_mask.shape[0]
    sign_inner = sign_mask.shape[2]
    col_blocks = sign_mask.shape[3]
    ring_count = lax.axis_size("y")
    pair_count = lax.axis_size("xlo")
    ring_me = lax.axis_index("y")
    pair_me = lax.axis_index("xlo")
    local_order = row_order[0]
    ks_panel = (
        ks_matrix.reshape(row_blocks, BS, inner_blocks, BS)
        * ks_mask.astype(jnp.bfloat16)[:, None, :, None]
    )
    ks_panel = jnp.take(ks_panel, local_order, axis=0, mode="clip")
    ks_split = ks_panel.reshape(ring_count, pair_count, BS, inner_blocks * BS)
    mine = lax.dynamic_index_in_dim(ks_split, pair_me, 1, keepdims=False)
    theirs = lax.dynamic_index_in_dim(ks_split, 1 - pair_me, 1, keepdims=False)
    lent = swap_with(theirs, "xlo", 1)
    payload = jnp.stack([mine, lent])
    payload = payload.reshape(pair_count, ring_count * BS, inner_blocks * BS)
    sign_kept = sign_matrix.reshape(local_groups, sign_inner, BS, col_blocks, BS)
    sign_kept = sign_kept * sign_mask.astype(jnp.bfloat16).reshape(
        local_groups, sign_inner, 1, col_blocks, 1
    )
    sign_kept = sign_kept.reshape(local_groups, sign_inner * BS, col_blocks * BS)
    me = lax.axis_index("col")
    chip_bit = me // 2
    core_bit = me % 2
    partner = swap_with(sign_kept, "xlo", 1)
    diag = swap_with(sign_kept, ("col", "xlo"), 5)
    far = swap_with(diag, "xlo", 1)
    mine_first = jnp.stack(
        [jnp.concatenate([sign_kept, far]), jnp.concatenate([partner, diag])]
    )
    far_first = jnp.stack(
        [jnp.concatenate([far, sign_kept]), jnp.concatenate([diag, partner])]
    )
    pair = jnp.where(chip_bit == 0, mine_first, far_first)
    near = swap_with(pair, "col", 1)
    core0 = jnp.where(core_bit == 0, pair, near)
    core1 = jnp.where(core_bit == 0, near, pair)
    shape = (pair_count, 2, local_groups, sign_inner * BS, col_blocks * BS)
    sign_four = jnp.stack([core0.reshape(shape), core1.reshape(shape)], axis=2)
    sign_four = sign_four.reshape(pair_count, -1, sign_inner * BS, col_blocks * BS)
    sign_four = jnp.swapaxes(sign_four, 0, 1)
    ks_whole = lax.all_gather(payload, "row", axis=0, tiled=False)
    product = jnp.einsum(
        "sjik,sjkn->in", ks_whole, sign_four, preferred_element_type=jnp.float32
    )
    parts = product.reshape(ring_count, BS, col_blocks * BS)
    arrived = lax.all_to_all(parts, "y", 0, 0, tiled=True)
    summed = jnp.sum(arrived, axis=0)
    own_row = lax.dynamic_index_in_dim(
        local_order, ring_me * pair_count + pair_me, 0, keepdims=False
    )
    own_mask = lax.dynamic_index_in_dim(product_mask, own_row, 0, keepdims=False)
    kept = summed.reshape(BS, col_blocks, BS) * own_mask.astype(jnp.float32)[None, :, None]
    return kept.reshape(BS, col_blocks * BS).astype(jnp.bfloat16)


def solution(mesh):
    rows, cols, depths = mesh.devices.shape
    pair_count = 2
    split_mesh = Mesh(
        mesh.devices.reshape(rows, cols, depths // pair_count, pair_count),
        ("row", "col", "y", "xlo"),
    )
    depth = ("y", "xlo")
    in_specs = (
        P("col", ("row", *depth)),
        P("col", depth, None, "row"),
        P("col", ("row", *depth)),
        P("col", depth, None, "row"),
        P("col", "row"),
        P("col", None),
    )
    out_specs = P(("col", *depth), "row")
    return jax.shard_map(
        per_device, mesh=split_mesh, in_specs=in_specs, out_specs=out_specs, check_vma=False
    )
```
